128 devices in a mesh: row: 8 (over x, core), cent: 16 (over y, z).
Axes of the slice: x: 4, y: 4, z: 4, core: 2. Of those that a mesh axis runs over, the one named last changes fastest.
Arguments:
- vectors: bfloat16 [16384, 768], P('row', 'cent'), may hold values from -6 to 6
- centroids: bfloat16 [16384, 768], P('cent'), may hold values from -6 to 6
- weights: float32 [16384], P('row'), may hold values from 1 to 270, as said below
Outputs:
- new_centroids: float32 [768, 16384], P('row', 'cent')
- row_log: float32 [16384], P('row')
- col_log: float32 [16384], P('cent')
The draws below stay inside these ranges and needn't reach their ends.
Inputs may be any that keep to these rules, and one draw needn't show every extreme that they name: Positive sample weights.
All inputs are finite; a program needn't handle non-finite values.
Results may differ from the reference program's by a relative error of at most 0.00082.
Values may be sent and summed in bfloat16 or wider, within the bound.
No kernel may reach another device: no remote copies, remote signals or barrier semaphores. Data moves between devices by JAX's collectives and lax.ppermute only.
A program may use at most 64 MiB of HBM per device.

```python
import math
import jax
import jax.numpy as jnp
from jax import lax

D = 768
K_DEV = 1024
ITERS = 3
N = 16384
K = 16384


shared_weight = 0.47


def drawn_directions(key):
    groups = K // K_DEV
    return jax.random.truncated_normal(jax.random.fold_in(key, 7), -3.0, 3.0, (groups, D), jnp.float32)


def vector_groups(key):
    groups = K // K_DEV
    return jax.random.randint(jax.random.fold_in(key, 11), (N,), 0, groups)


def draw_vectors(key, part):
    member = vector_groups(key)
    directions = drawn_directions(key)
    noise = jax.random.truncated_normal(jax.random.fold_in(key, 17), -4.0, 4.0, (N, D), jnp.float32)
    return (shared_weight * directions[member] + noise).astype(jnp.bfloat16)


def draw_centroids(key, part):
    directions = jnp.repeat(drawn_directions(key), K_DEV, axis=0)
    noise = jax.random.truncated_normal(jax.random.fold_in(key, 23), -4.0, 4.0, (K, D), jnp.float32)
    return (shared_weight * directions + noise).astype(jnp.bfloat16)


def draw_weights(key, part):
    groups = K // K_DEV
    member = vector_groups(key)
    factor_draw = jax.random.uniform(jax.random.fold_in(key, 13), (groups,), jnp.float32, 0.0, 1.0)
    factors = jnp.exp(factor_draw * jnp.log(3.0))[member]
    tile_cursor = jnp.arange(N).astype(jnp.float32) / max(N - 1, 1)
    spread = jax.random.uniform(key, (N,), jnp.float32, 0.0, 1.0)
    base = jnp.exp(spread * jnp.log(10.0))
    return base * (1.0 + 2.0 * tile_cursor) * factors


def setup_inputs(seed: int = 0) -> dict:
    arg_keys = jax.random.split(jax.random.key(seed), 4)
    vectors = draw_vectors(jax.random.fold_in(arg_keys[3], 71), 0)
    centroids = draw_centroids(jax.random.fold_in(arg_keys[3], 71), 0)
    weights = draw_weights(jax.random.fold_in(arg_keys[3], 71), 0)
    return dict(vectors=vectors, centroids=centroids, weights=weights)


entropic_smoothing = 0.02

def reference(vectors, centroids, weights):
    total_rows = vectors.shape[0]
    feature_dimension = vectors.shape[1]
    centre_total = centroids.shape[0]
    block_rows = math.gcd(total_rows, 1024)
    block_count = total_rows // block_rows
    reciprocal_vector_magnitudes = lax.rsqrt(lax.optimization_barrier(jnp.mean(jnp.square(vectors.astype(jnp.float32)), axis=1)) + 1e-06)
    reciprocal_centroid_magnitudes = lax.rsqrt(lax.optimization_barrier(jnp.mean(jnp.square(centroids.astype(jnp.float32)), axis=1)) + 1e-06)

    def kernel_rows(inputs):
        vec_block, reciprocal_magnitude_tile = inputs
        similarity_matrix = jnp.dot(vec_block, centroids.T, preferred_element_type=jnp.float32)
        sharpened_similarity = similarity_matrix * reciprocal_magnitude_tile[:, None] * reciprocal_centroid_magnitudes[None, :] / (feature_dimension * entropic_smoothing)
        return jnp.exp(sharpened_similarity).astype(jnp.bfloat16)
    vec_blocks = vectors.reshape(block_count, block_rows, feature_dimension)
    kernel = lax.map(kernel_rows, (vec_blocks, reciprocal_vector_magnitudes.reshape(block_count, block_rows)))
    weight_blocks = weights.reshape(block_count, block_rows)
    weight_sum = jnp.sum(weights)

    def row_step(col_scale):
        masses = lax.map(lambda kern_block: lax.optimization_barrier(jnp.sum(kern_block.astype(jnp.float32) * col_scale[None, :], axis=1)), kernel)
        return weight_blocks / masses

    def col_step(row_scale):

        def block_mass(paired):
            return lax.optimization_barrier(jnp.sum(paired[0].astype(jnp.float32) * paired[1][:, None], axis=0))
        masses = lax.optimization_barrier(jnp.sum(lax.map(block_mass, (kernel, row_scale)), axis=0))
        return weight_sum / centre_total / masses
    col_scale = jnp.full((centre_total,), 1.0, jnp.float32) / centre_total
    row_scale = row_step(col_scale)
    for sweep in range(ITERS):
        col_scale = col_step(row_scale)
        row_scale = row_step(col_scale)

    def accumulate(carry, inputs):
        kern_block, scale_block, vec_block = inputs
        transport = (scale_block[:, None] * kern_block.astype(jnp.float32) * col_scale[None, :]).astype(jnp.bfloat16)
        term = lax.dot_general(vec_block, transport, (((0,), (0,)), ((), ())), preferred_element_type=jnp.float32)
        return (carry + term, None)
    start_sum = jnp.zeros((feature_dimension, centre_total), jnp.float32)
    summed, unused = lax.scan(accumulate, start_sum, (kernel, row_scale, vec_blocks))
    new_centroids = summed * lax.rsqrt(lax.optimization_barrier(jnp.mean(summed * summed, axis=0)) + 1e-06)[None, :]
    return (new_centroids, jnp.log(row_scale.reshape(-1)), jnp.log(centre_total * col_scale))
```

```python
import math

import jax
import jax.numpy as jnp
from jax import lax
from jax.sharding import Mesh
from jax.sharding import PartitionSpec as P

ITERS = 3


entropic_smoothing = 0.02

ROW = ("rx", "rc")
CENT = ("cy", "cz")


def shifted_sum(x, axis):
    n = lax.axis_size(axis)
    total = x
    for k in range(1, n):
        total = total + lax.ppermute(x, axis, [(i, (i + k) % n) for i in range(n)])
    return total


def reduce_cent(x):
    return shifted_sum(shifted_sum(x, "cz"), "cy")


def reduce_row(x):
    return shifted_sum(shifted_sum(x, "rc"), "rx")


def scatter_row(x):
    n = lax.axis_size(ROW)
    me = lax.axis_index(ROW)
    blocks = x.reshape(n, x.shape[0] // n, *x.shape[1:])
    total = lax.dynamic_index_in_dim(blocks, me, 0, keepdims=False)
    for k in range(1, n):
        piece = lax.dynamic_index_in_dim(blocks, (me + k) % n, 0, keepdims=False)
        total = total + lax.ppermute(piece, ROW, [(i, (i + k) % n) for i in range(n)])
    return total


def row_step(kernel, col_scale, weights):
    partial_mass = jnp.sum(kernel.astype(jnp.float32) * col_scale[None, :], axis=1)
    masses = reduce_cent(partial_mass)
    return weights / masses


def per_device(vectors, centroids, weights):
    full_rows = lax.all_gather(vectors, CENT, axis=1, tiled=True)
    local_rows = full_rows.shape[0]
    feature_dimension = full_rows.shape[1]
    local_centres = centroids.shape[0]
    centre_total = local_centres * lax.axis_size(CENT)
    block_rows = math.gcd(local_rows, 512)
    block_count = local_rows // block_rows
    reciprocal_vector_magnitudes = lax.rsqrt(
        jnp.mean(jnp.square(full_rows.astype(jnp.float32)), axis=1) + 1e-06
    )
    reciprocal_centroid_magnitudes = lax.rsqrt(
        jnp.mean(jnp.square(centroids.astype(jnp.float32)), axis=1) + 1e-06
    )

    def kernel_rows(inputs):
        vec_block, reciprocal_magnitude_tile = inputs
        similarity_matrix = jnp.dot(vec_block, centroids.T, preferred_element_type=jnp.float32)
        sharpened_similarity = (
            similarity_matrix
            * reciprocal_magnitude_tile[:, None]
            * reciprocal_centroid_magnitudes[None, :]
            / (feature_dimension * entropic_smoothing)
        )
        return jnp.exp(sharpened_similarity).astype(jnp.bfloat16)

    kernel = lax.map(
        kernel_rows,
        (
            full_rows.reshape(block_count, block_rows, feature_dimension),
            reciprocal_vector_magnitudes.reshape(block_count, block_rows),
        ),
    )
    kernel = kernel.reshape(local_rows, local_centres)
    weight_sum = reduce_row(jnp.sum(weights))
    col_scale = jnp.full((local_centres,), 1.0, jnp.float32) / centre_total
    row_scale = row_step(kernel, col_scale, weights)
    for sweep in range(ITERS):
        partial_cols = jnp.sum(kernel.astype(jnp.float32) * row_scale[:, None], axis=0)
        col_mass = reduce_row(partial_cols)
        col_scale = weight_sum / centre_total / col_mass
        row_scale = row_step(kernel, col_scale, weights)
    transport = (row_scale[:, None] * kernel.astype(jnp.float32) * col_scale[None, :]).astype(
        jnp.bfloat16
    )
    term = lax.dot_general(
        full_rows, transport, (((0,), (0,)), ((), ())), preferred_element_type=jnp.float32
    )
    own_summed = scatter_row(term)
    square_sum = reduce_row(jnp.sum(own_summed * own_summed, axis=0))
    new_centroids = own_summed * lax.rsqrt(square_sum / feature_dimension + 1e-06)[None, :]
    return (new_centroids, jnp.log(row_scale), jnp.log(centre_total * col_scale))


def solution(mesh):
    rows, cents = mesh.devices.shape
    split = Mesh(mesh.devices.reshape(rows // 2, 2, 4, cents // 4), ROW + CENT)
    return jax.shard_map(
        per_device,
        mesh=split,
        in_specs=(P(ROW, CENT), P(CENT, None), P(ROW)),
        out_specs=(P(ROW, CENT), P(ROW), P(CENT)),
        check_vma=False,
    )
```

```python
import jax
import jax.numpy as jnp
from jax import lax
from jax.sharding import Mesh
from jax.sharding import PartitionSpec as P

ITERS = 3


entropic_smoothing = 0.02

ROW = ("rx", "rc")
CENT = ("cy", "cz")


def shifted_sum(x, axis):
    n = lax.axis_size(axis)
    total = x
    for k in range(1, n):
        total = total + lax.ppermute(x, axis, [(i, (i + k) % n) for i in range(n)])
    return total


def reduce_cent(x):
    return shifted_sum(shifted_sum(x, "cz"), "cy")


def reduce_row(x):
    return shifted_sum(shifted_sum(x, "rc"), "rx")


def scatter_row(x):
    chips, cores = lax.axis_size("rx"), lax.axis_size("rc")
    rx, rc = lax.axis_index("rx"), lax.axis_index("rc")
    blocks = x.reshape(chips, cores, x.shape[0] // (chips * cores), *x.shape[1:])
    half = lax.dynamic_index_in_dim(blocks, rc, 1, keepdims=False)
    for k in range(1, cores):
        piece = lax.dynamic_index_in_dim(blocks, (rc + k) % cores, 1, keepdims=False)
        half = half + lax.ppermute(piece, "rc", [(i, (i + k) % cores) for i in range(cores)])
    total = lax.dynamic_index_in_dim(half, rx, 0, keepdims=False)
    for k in range(1, chips):
        piece = lax.dynamic_index_in_dim(half, (rx + k) % chips, 0, keepdims=False)
        total = total + lax.ppermute(piece, "rx", [(i, (i + k) % chips) for i in range(chips)])
    return total


def row_step(kernel, col_scale, weights):
    partial_mass = jnp.sum(kernel.astype(jnp.float32) * col_scale[None, :], axis=1)
    masses = reduce_cent(partial_mass)
    return weights / masses


def per_device(vectors, centroids, weights):
    full_rows = lax.all_gather(vectors, CENT, axis=1, tiled=True)
    local_rows = full_rows.shape[0]
    feature_dimension = full_rows.shape[1]
    local_centres = centroids.shape[0]
    centre_total = local_centres * lax.axis_size(CENT)
    reciprocal_vector_magnitudes = lax.rsqrt(
        jnp.mean(jnp.square(full_rows.astype(jnp.float32)), axis=1) + 1e-06
    )
    reciprocal_centroid_magnitudes = lax.rsqrt(
        jnp.mean(jnp.square(centroids.astype(jnp.float32)), axis=1) + 1e-06
    )
    similarity_matrix = jnp.dot(full_rows, centroids.T, preferred_element_type=jnp.float32)
    sharpened_similarity = (
        similarity_matrix
        * reciprocal_vector_magnitudes[:, None]
        * reciprocal_centroid_magnitudes[None, :]
        / (feature_dimension * entropic_smoothing)
    )
    kernel = jnp.exp(sharpened_similarity).astype(jnp.bfloat16)
    weight_sum = reduce_row(jnp.sum(weights))
    col_scale = jnp.full((local_centres,), 1.0, jnp.float32) / centre_total
    row_scale = row_step(kernel, col_scale, weights)
    for sweep in range(ITERS):
        partial_cols = jnp.sum(kernel.astype(jnp.float32) * row_scale[:, None], axis=0)
        col_mass = reduce_row(partial_cols)
        col_scale = weight_sum / centre_total / col_mass
        row_scale = row_step(kernel, col_scale, weights)
    transport = (row_scale[:, None] * kernel.astype(jnp.float32) * col_scale[None, :]).astype(
        jnp.bfloat16
    )
    term = lax.dot_general(
        full_rows, transport, (((0,), (0,)), ((), ())), preferred_element_type=jnp.float32
    )
    own_summed = scatter_row(term)
    square_sum = reduce_row(jnp.sum(own_summed * own_summed, axis=0))
    new_centroids = own_summed * lax.rsqrt(square_sum / feature_dimension + 1e-06)[None, :]
    return (new_centroids, jnp.log(row_scale), jnp.log(centre_total * col_scale))


def solution(mesh):
    rows, cents = mesh.devices.shape
    split = Mesh(mesh.devices.reshape(rows // 2, 2, 4, cents // 4), ROW + CENT)
    return jax.shard_map(
        per_device,
        mesh=split,
        in_specs=(P(ROW, CENT), P(CENT, None), P(ROW)),
        out_specs=(P(ROW, CENT), P(ROW), P(CENT)),
        check_vma=False,
    )
```

```python
import jax
import jax.numpy as jnp
from jax import lax
from jax.sharding import Mesh
from jax.sharding import PartitionSpec as P

ITERS = 3


entropic_smoothing = 0.02

ROW = ("rx", "rc")
CENT = ("cy", "cz")


def shifted_sum(x, axis):
    n = lax.axis_size(axis)
    total = x
    for k in range(1, n):
        total = total + lax.ppermute(x, axis, [(i, (i + k) % n) for i in range(n)])
    return total


def reduce_cent(x):
    n = lax.axis_size(CENT)
    copies = lax.all_to_all(jnp.broadcast_to(x, (n, *x.shape)), CENT, 0, 0, tiled=False)
    return jnp.sum(copies, axis=0)


def reduce_row(x):
    return shifted_sum(shifted_sum(x, "rc"), "rx")


def scatter_row(x):
    chips, cores = lax.axis_size("rx"), lax.axis_size("rc")
    rx, rc = lax.axis_index("rx"), lax.axis_index("rc")
    blocks = x.reshape(chips, cores, x.shape[0] // (chips * cores), *x.shape[1:])
    half = lax.dynamic_index_in_dim(blocks, rc, 1, keepdims=False)
    for k in range(1, cores):
        piece = lax.dynamic_index_in_dim(blocks, (rc + k) % cores, 1, keepdims=False)
        half = half + lax.ppermute(piece, "rc", [(i, (i + k) % cores) for i in range(cores)])
    total = lax.dynamic_index_in_dim(half, rx, 0, keepdims=False)
    for k in range(1, chips):
        piece = lax.dynamic_index_in_dim(half, (rx + k) % chips, 0, keepdims=False)
        total = total + lax.ppermute(piece, "rx", [(i, (i + k) % chips) for i in range(chips)])
    return total


def row_step(kernel, col_scale, weights):
    partial_mass = jnp.sum(kernel.astype(jnp.float32) * col_scale[None, :], axis=1)
    masses = reduce_cent(partial_mass)
    return weights / masses


def per_device(vectors, centroids, weights):
    full_rows = lax.all_gather(vectors, CENT, axis=1, tiled=True)
    local_rows = full_rows.shape[0]
    feature_dimension = full_rows.shape[1]
    local_centres = centroids.shape[0]
    centre_total = local_centres * lax.axis_size(CENT)
    reciprocal_vector_magnitudes = lax.rsqrt(
        jnp.mean(jnp.square(full_rows.astype(jnp.float32)), axis=1) + 1e-06
    )
    reciprocal_centroid_magnitudes = lax.rsqrt(
        jnp.mean(jnp.square(centroids.astype(jnp.float32)), axis=1) + 1e-06
    )
    similarity_matrix = jnp.dot(full_rows, centroids.T, preferred_element_type=jnp.float32)
    sharpened_similarity = (
        similarity_matrix
        * reciprocal_vector_magnitudes[:, None]
        * reciprocal_centroid_magnitudes[None, :]
        / (feature_dimension * entropic_smoothing)
    )
    kernel = jnp.exp(sharpened_similarity).astype(jnp.bfloat16)
    weight_sum = reduce_row(jnp.sum(weights))
    col_scale = jnp.full((local_centres,), 1.0, jnp.float32) / centre_total
    row_scale = row_step(kernel, col_scale, weights)
    for sweep in range(ITERS):
        partial_cols = jnp.sum(kernel.astype(jnp.float32) * row_scale[:, None], axis=0)
        col_mass = reduce_row(partial_cols)
        col_scale = weight_sum / centre_total / col_mass
        row_scale = row_step(kernel, col_scale, weights)
    transport = (row_scale[:, None] * kernel.astype(jnp.float32) * col_scale[None, :]).astype(
        jnp.bfloat16
    )
    term = lax.dot_general(
        full_rows, transport, (((0,), (0,)), ((), ())), preferred_element_type=jnp.float32
    )
    own_summed = scatter_row(term)
    square_sum = reduce_row(jnp.sum(own_summed * own_summed, axis=0))
    new_centroids = own_summed * lax.rsqrt(square_sum / feature_dimension + 1e-06)[None, :]
    return (new_centroids, jnp.log(row_scale), jnp.log(centre_total * col_scale))


def solution(mesh):
    rows, cents = mesh.devices.shape
    split = Mesh(mesh.devices.reshape(rows // 2, 2, 4, cents // 4), ROW + CENT)
    return jax.shard_map(
        per_device,
        mesh=split,
        in_specs=(P(ROW, CENT), P(CENT, None), P(ROW)),
        out_specs=(P(ROW, CENT), P(ROW), P(CENT)),
        check_vma=False,
    )
```

```python
import jax
import jax.numpy as jnp
from jax import lax
from jax.sharding import Mesh
from jax.sharding import PartitionSpec as P

ITERS = 3


entropic_smoothing = 0.02

ROW = ("rx", "rc")
CENT = ("cy", "cz")


def shifted_sum(x, axis):
    n = lax.axis_size(axis)
    total = x
    for k in range(1, n):
        total = total + lax.ppermute(x, axis, [(i, (i + k) % n) for i in range(n)])
    return total


def reduce_cent(x):
    n = lax.axis_size(CENT)
    copies = lax.all_to_all(jnp.broadcast_to(x, (n, *x.shape)), CENT, 0, 0, tiled=False)
    return jnp.sum(copies, axis=0)


def reduce_row(x):
    return shifted_sum(shifted_sum(x, "rc"), "rx")


def scatter_row(x):
    chips, cores = lax.axis_size("rx"), lax.axis_size("rc")
    rx, rc = lax.axis_index("rx"), lax.axis_index("rc")
    blocks = x.reshape(chips, cores, x.shape[0] // (chips * cores), *x.shape[1:])
    half = lax.dynamic_index_in_dim(blocks, rc, 1, keepdims=False)
    for k in range(1, cores):
        piece = lax.dynamic_index_in_dim(blocks, (rc + k) % cores, 1, keepdims=False)
        half = half + lax.ppermute(piece, "rc", [(i, (i + k) % cores) for i in range(cores)])
    total = lax.dynamic_index_in_dim(half, rx, 0, keepdims=False)
    for k in range(1, chips):
        piece = lax.dynamic_index_in_dim(half, (rx + k) % chips, 0, keepdims=False)
        total = total + lax.ppermute(piece, "rx", [(i, (i + k) % chips) for i in range(chips)])
    return total


def row_step(kernel, col_scale, weights):
    partial_mass = jnp.sum(kernel.astype(jnp.float32) * col_scale[None, :], axis=1)
    masses = reduce_cent(partial_mass)
    return weights / masses


def per_device(vectors, centroids, weights):
    full_rows = lax.all_gather(vectors, CENT, axis=1, tiled=True)
    local_rows = full_rows.shape[0]
    feature_dimension = full_rows.shape[1]
    local_centres = centroids.shape[0]
    centre_total = local_centres * lax.axis_size(CENT)
    reciprocal_vector_magnitudes = lax.rsqrt(
        jnp.mean(jnp.square(full_rows.astype(jnp.float32)), axis=1) + 1e-06
    )
    reciprocal_centroid_magnitudes = lax.rsqrt(
        jnp.mean(jnp.square(centroids.astype(jnp.float32)), axis=1) + 1e-06
    )
    similarity_matrix = jnp.dot(full_rows, centroids.T, preferred_element_type=jnp.float32)
    sharpened_similarity = (
        similarity_matrix
        * reciprocal_vector_magnitudes[:, None]
        * reciprocal_centroid_magnitudes[None, :]
        / (feature_dimension * entropic_smoothing)
    )
    kernel = jnp.exp(sharpened_similarity).astype(jnp.bfloat16)
    col_scale = jnp.full((local_centres,), 1.0, jnp.float32) / centre_total
    row_scale = row_step(kernel, col_scale, weights)
    weight_sum = None
    for sweep in range(ITERS):
        partial_cols = jnp.sum(kernel.astype(jnp.float32) * row_scale[:, None], axis=0)
        if weight_sum is None:
            both = reduce_row(jnp.concatenate([partial_cols, jnp.sum(weights)[None]]))
            col_mass, weight_sum = both[:local_centres], both[local_centres]
        else:
            col_mass = reduce_row(partial_cols)
        col_scale = weight_sum / centre_total / col_mass
        row_scale = row_step(kernel, col_scale, weights)
    transport = (row_scale[:, None] * kernel.astype(jnp.float32) * col_scale[None, :]).astype(
        jnp.bfloat16
    )
    term = lax.dot_general(
        full_rows, transport, (((0,), (0,)), ((), ())), preferred_element_type=jnp.float32
    )
    own_summed = scatter_row(term)
    square_sum = reduce_row(jnp.sum(own_summed * own_summed, axis=0))
    new_centroids = own_summed * lax.rsqrt(square_sum / feature_dimension + 1e-06)[None, :]
    return (new_centroids, jnp.log(row_scale), jnp.log(centre_total * col_scale))


def solution(mesh):
    rows, cents = mesh.devices.shape
    split = Mesh(mesh.devices.reshape(rows // 2, 2, 4, cents // 4), ROW + CENT)
    return jax.shard_map(
        per_device,
        mesh=split,
        in_specs=(P(ROW, CENT), P(CENT, None), P(ROW)),
        out_specs=(P(ROW, CENT), P(ROW), P(CENT)),
        check_vma=False,
    )
```

```python
import jax
import jax.numpy as jnp
from jax import lax
from jax.sharding import Mesh
from jax.sharding import PartitionSpec as P

ITERS = 3


entropic_smoothing = 0.02

ROW = ("rx", "rc")
CENT = ("cy", "cz")


def shifted_sum(x, axis):
    n = lax.axis_size(axis)
    total = x
    for k in range(1, n):
        total = total + lax.ppermute(x, axis, [(i, (i + k) % n) for i in range(n)])
    return total


def reduce_cent(x):
    n = lax.axis_size(CENT)
    copies = lax.all_to_all(jnp.broadcast_to(x, (n, *x.shape)), CENT, 0, 0, tiled=False)
    return jnp.sum(copies, axis=0)


def reduce_row(x):
    return shifted_sum(shifted_sum(x, "rc"), "rx")


def scatter_row(x):
    chips, cores = lax.axis_size("rx"), lax.axis_size("rc")
    rx, rc = lax.axis_index("rx"), lax.axis_index("rc")
    blocks = x.reshape(chips, cores, x.shape[0] // (chips * cores), *x.shape[1:])
    half = lax.dynamic_index_in_dim(blocks, rc, 1, keepdims=False)
    for k in range(1, cores):
        piece = lax.dynamic_index_in_dim(blocks, (rc + k) % cores, 1, keepdims=False)
        half = half + lax.ppermute(piece, "rc", [(i, (i + k) % cores) for i in range(cores)])
    total = lax.dynamic_index_in_dim(half, rx, 0, keepdims=False)
    for k in range(1, chips):
        piece = lax.dynamic_index_in_dim(half, (rx + k) % chips, 0, keepdims=False)
        total = total + lax.ppermute(piece, "rx", [(i, (i + k) % chips) for i in range(chips)])
    return total


def row_step(kernel, col_scale, weights):
    partial_mass = jnp.sum(kernel.astype(jnp.float32) * col_scale[None, :], axis=1)
    masses = reduce_cent(partial_mass)
    return weights / masses


def per_device(vectors, centroids, weights):
    full_rows = lax.all_gather(vectors, CENT, axis=1, tiled=True)
    local_rows = full_rows.shape[0]
    feature_dimension = full_rows.shape[1]
    local_centres = centroids.shape[0]
    centre_total = local_centres * lax.axis_size(CENT)
    reciprocal_vector_magnitudes = lax.rsqrt(
        jnp.mean(jnp.square(full_rows.astype(jnp.float32)), axis=1) + 1e-06
    )
    reciprocal_centroid_magnitudes = lax.rsqrt(
        jnp.mean(jnp.square(centroids.astype(jnp.float32)), axis=1) + 1e-06
    )
    similarity_matrix = jnp.dot(full_rows, centroids.T, preferred_element_type=jnp.float32)
    sharpened_similarity = (
        similarity_matrix
        * reciprocal_vector_magnitudes[:, None]
        * reciprocal_centroid_magnitudes[None, :]
        / (feature_dimension * entropic_smoothing)
    )
    kernel = jnp.exp(sharpened_similarity).astype(jnp.bfloat16)
    col_scale = jnp.full((local_centres,), 1.0, jnp.float32) / centre_total
    row_scale = row_step(kernel, col_scale, weights)
    weight_sum = None
    for sweep in range(ITERS):
        partial_cols = jnp.sum(kernel.astype(jnp.float32) * row_scale[:, None], axis=0)
        if weight_sum is None:
            both = reduce_row(jnp.concatenate([partial_cols, jnp.sum(weights)[None]]))
            col_mass, weight_sum = both[:local_centres], both[local_centres]
        else:
            col_mass = reduce_row(partial_cols)
        col_scale = weight_sum / centre_total / col_mass
        row_scale = row_step(kernel, col_scale, weights)
    halves = 2
    width = local_centres // halves
    pieces = []
    for half in range(halves):
        columns = slice(half * width, (half + 1) * width)
        transport = (
            row_scale[:, None] * kernel[:, columns].astype(jnp.float32) * col_scale[None, columns]
        ).astype(jnp.bfloat16)
        term = lax.dot_general(
            full_rows, transport, (((0,), (0,)), ((), ())), preferred_element_type=jnp.float32
        )
        own_summed = scatter_row(term)
        square_sum = reduce_row(jnp.sum(own_summed * own_summed, axis=0))
        pieces.append(own_summed * lax.rsqrt(square_sum / feature_dimension + 1e-06)[None, :])
    new_centroids = jnp.concatenate(pieces, axis=1)
    return (new_centroids, jnp.log(row_scale), jnp.log(centre_total * col_scale))


def solution(mesh):
    rows, cents = mesh.devices.shape
    split = Mesh(mesh.devices.reshape(rows // 2, 2, 4, cents // 4), ROW + CENT)
    return jax.shard_map(
        per_device,
        mesh=split,
        in_specs=(P(ROW, CENT), P(CENT, None), P(ROW)),
        out_specs=(P(ROW, CENT), P(ROW), P(CENT)),
        check_vma=False,
    )
```

```python
import jax
import jax.numpy as jnp
from jax import lax
from jax.sharding import Mesh
from jax.sharding import PartitionSpec as P

ITERS = 3


entropic_smoothing = 0.02

ROW = ("rx", "rc")
CENT = ("cy", "cz")


def shifted_sum(x, axis):
    n = lax.axis_size(axis)
    total = x
    for k in range(1, n):
        total = total + lax.ppermute(x, axis, [(i, (i + k) % n) for i in range(n)])
    return total


def reduce_cent(x):
    n = lax.axis_size(CENT)
    copies = lax.all_to_all(jnp.broadcast_to(x, (n, *x.shape)), CENT, 0, 0, tiled=False)
    return jnp.sum(copies, axis=0)


def reduce_row(x):
    n = lax.axis_size(ROW)
    copies = lax.all_to_all(jnp.broadcast_to(x, (n, *x.shape)), ROW, 0, 0, tiled=False)
    return jnp.sum(copies, axis=0)


def scatter_row(x):
    chips, cores = lax.axis_size("rx"), lax.axis_size("rc")
    rx, rc = lax.axis_index("rx"), lax.axis_index("rc")
    blocks = x.reshape(chips, cores, x.shape[0] // (chips * cores), *x.shape[1:])
    half = lax.dynamic_index_in_dim(blocks, rc, 1, keepdims=False)
    for k in range(1, cores):
        piece = lax.dynamic_index_in_dim(blocks, (rc + k) % cores, 1, keepdims=False)
        half = half + lax.ppermute(piece, "rc", [(i, (i + k) % cores) for i in range(cores)])
    return jnp.sum(lax.all_to_all(half, "rx", 0, 0, tiled=False), axis=0)


def row_step(kernel, col_scale, weights):
    partial_mass = jnp.sum(kernel.astype(jnp.float32) * col_scale[None, :], axis=1)
    masses = reduce_cent(partial_mass)
    return weights / masses


def per_device(vectors, centroids, weights):
    full_rows = lax.all_gather(vectors, CENT, axis=1, tiled=True)
    local_rows = full_rows.shape[0]
    feature_dimension = full_rows.shape[1]
    local_centres = centroids.shape[0]
    centre_total = local_centres * lax.axis_size(CENT)
    reciprocal_vector_magnitudes = lax.rsqrt(
        jnp.mean(jnp.square(full_rows.astype(jnp.float32)), axis=1) + 1e-06
    )
    reciprocal_centroid_magnitudes = lax.rsqrt(
        jnp.mean(jnp.square(centroids.astype(jnp.float32)), axis=1) + 1e-06
    )
    similarity_matrix = jnp.dot(full_rows, centroids.T, preferred_element_type=jnp.float32)
    sharpened_similarity = (
        similarity_matrix
        * reciprocal_vector_magnitudes[:, None]
        * reciprocal_centroid_magnitudes[None, :]
        / (feature_dimension * entropic_smoothing)
    )
    kernel = jnp.exp(sharpened_similarity).astype(jnp.bfloat16)
    col_scale = jnp.full((local_centres,), 1.0, jnp.float32) / centre_total
    row_scale = row_step(kernel, col_scale, weights)
    weight_sum = None
    for sweep in range(ITERS):
        partial_cols = jnp.sum(kernel.astype(jnp.float32) * row_scale[:, None], axis=0)
        if weight_sum is None:
            both = reduce_row(jnp.concatenate([partial_cols, jnp.sum(weights)[None]]))
            col_mass, weight_sum = both[:local_centres], both[local_centres]
        else:
            col_mass = reduce_row(partial_cols)
        col_scale = weight_sum / centre_total / col_mass
        row_scale = row_step(kernel, col_scale, weights)
    transport = (row_scale[:, None] * kernel.astype(jnp.float32) * col_scale[None, :]).astype(
        jnp.bfloat16
    )
    term = lax.dot_general(
        full_rows, transport, (((0,), (0,)), ((), ())), preferred_element_type=jnp.float32
    )
    own_summed = scatter_row(term)
    square_sum = reduce_row(jnp.sum(own_summed * own_summed, axis=0))
    new_centroids = own_summed * lax.rsqrt(square_sum / feature_dimension + 1e-06)[None, :]
    return (new_centroids, jnp.log(row_scale), jnp.log(centre_total * col_scale))


def solution(mesh):
    rows, cents = mesh.devices.shape
    split = Mesh(mesh.devices.reshape(rows // 2, 2, 4, cents // 4), ROW + CENT)
    return jax.shard_map(
        per_device,
        mesh=split,
        in_specs=(P(ROW, CENT), P(CENT, None), P(ROW)),
        out_specs=(P(ROW, CENT), P(ROW), P(CENT)),
        check_vma=False,
    )
```

```python
import jax
import jax.numpy as jnp
from jax import lax
from jax.sharding import Mesh
from jax.sharding import PartitionSpec as P

ITERS = 3


entropic_smoothing = 0.02

ROW = ("rx", "rc")
CENT = ("cy", "cz")


def shifted_sum(x, axis):
    n = lax.axis_size(axis)
    total = x
    for k in range(1, n):
        total = total + lax.ppermute(x, axis, [(i, (i + k) % n) for i in range(n)])
    return total


def reduce_cent(x):
    n = lax.axis_size(CENT)
    copies = lax.all_to_all(jnp.broadcast_to(x, (n, *x.shape)), CENT, 0, 0, tiled=False)
    return jnp.sum(copies, axis=0)


def reduce_row(x):
    n = lax.axis_size(ROW)
    copies = lax.all_to_all(jnp.broadcast_to(x, (n, *x.shape)), ROW, 0, 0, tiled=False)
    return jnp.sum(copies, axis=0)


def scatter_row(x):
    chips, cores = lax.axis_size("rx"), lax.axis_size("rc")
    rx, rc = lax.axis_index("rx"), lax.axis_index("rc")
    blocks = x.reshape(chips, cores, x.shape[0] // (chips * cores), *x.shape[1:])
    half = lax.dynamic_index_in_dim(blocks, rc, 1, keepdims=False)
    for k in range(1, cores):
        piece = lax.dynamic_index_in_dim(blocks, (rc + k) % cores, 1, keepdims=False)
        half = half + lax.ppermute(piece, "rc", [(i, (i + k) % cores) for i in range(cores)])
    total = lax.dynamic_index_in_dim(half, rx, 0, keepdims=False)
    for k in range(1, chips):
        piece = lax.dynamic_index_in_dim(half, (rx + k) % chips, 0, keepdims=False)
        total = total + lax.ppermute(piece, "rx", [(i, (i + k) % chips) for i in range(chips)])
    return total


def row_step(kernel, col_scale, weights):
    partial_mass = jnp.sum(kernel.astype(jnp.float32) * col_scale[None, :], axis=1)
    masses = reduce_cent(partial_mass)
    return lax.optimization_barrier(weights / masses)


def per_device(vectors, centroids, weights):
    full_rows = lax.all_gather(vectors, CENT, axis=1, tiled=True)
    local_rows = full_rows.shape[0]
    feature_dimension = full_rows.shape[1]
    local_centres = centroids.shape[0]
    centre_total = local_centres * lax.axis_size(CENT)
    reciprocal_vector_magnitudes = lax.rsqrt(
        jnp.mean(jnp.square(full_rows.astype(jnp.float32)), axis=1) + 1e-06
    )
    reciprocal_centroid_magnitudes = lax.rsqrt(
        jnp.mean(jnp.square(centroids.astype(jnp.float32)), axis=1) + 1e-06
    )
    similarity_matrix = jnp.dot(full_rows, centroids.T, preferred_element_type=jnp.float32)
    sharpened_similarity = (
        similarity_matrix
        * reciprocal_vector_magnitudes[:, None]
        * reciprocal_centroid_magnitudes[None, :]
        / (feature_dimension * entropic_smoothing)
    )
    kernel = jnp.exp(sharpened_similarity).astype(jnp.bfloat16)
    col_scale = jnp.full((local_centres,), 1.0, jnp.float32) / centre_total
    row_scale = row_step(kernel, col_scale, weights)
    weight_sum = None
    for sweep in range(ITERS):
        partial_cols = jnp.sum(kernel.astype(jnp.float32) * row_scale[:, None], axis=0)
        if weight_sum is None:
            both = reduce_row(jnp.concatenate([partial_cols, jnp.sum(weights)[None]]))
            col_mass, weight_sum = both[:local_centres], both[local_centres]
        else:
            col_mass = reduce_row(partial_cols)
        col_scale = lax.optimization_barrier(weight_sum / centre_total / col_mass)
        row_scale = row_step(kernel, col_scale, weights)
    transport = (row_scale[:, None] * kernel.astype(jnp.float32) * col_scale[None, :]).astype(
        jnp.bfloat16
    )
    term = lax.dot_general(
        full_rows, transport, (((0,), (0,)), ((), ())), preferred_element_type=jnp.float32
    )
    own_summed = scatter_row(term)
    square_sum = reduce_row(jnp.sum(own_summed * own_summed, axis=0))
    new_centroids = own_summed * lax.rsqrt(square_sum / feature_dimension + 1e-06)[None, :]
    return (new_centroids, jnp.log(row_scale), jnp.log(centre_total * col_scale))


def solution(mesh):
    rows, cents = mesh.devices.shape
    split = Mesh(mesh.devices.reshape(rows // 2, 2, 4, cents // 4), ROW + CENT)
    return jax.shard_map(
        per_device,
        mesh=split,
        in_specs=(P(ROW, CENT), P(CENT, None), P(ROW)),
        out_specs=(P(ROW, CENT), P(ROW), P(CENT)),
        check_vma=False,
    )
```

```python
import jax
import jax.numpy as jnp
from jax import lax
from jax.sharding import Mesh
from jax.sharding import PartitionSpec as P

ITERS = 3


entropic_smoothing = 0.02

ROW = ("rx", "rc")
CENT = ("cy", "cz")


def shifted_sum(x, axis):
    n = lax.axis_size(axis)
    total = x
    for k in range(1, n):
        total = total + lax.ppermute(x, axis, [(i, (i + k) % n) for i in range(n)])
    return total


def reduce_cent(x):
    n = lax.axis_size(CENT)
    copies = lax.all_to_all(jnp.broadcast_to(x, (n, *x.shape)), CENT, 0, 0, tiled=False)
    return jnp.sum(copies, axis=0)


def reduce_row(x):
    return shifted_sum(shifted_sum(x, "rc"), "rx")


def scatter_row(x):
    chips, cores = lax.axis_size("rx"), lax.axis_size("rc")
    rx, rc = lax.axis_index("rx"), lax.axis_index("rc")
    blocks = x.reshape(chips, cores, x.shape[0] // (chips * cores), *x.shape[1:])
    half = lax.dynamic_index_in_dim(blocks, rc, 1, keepdims=False)
    for k in range(1, cores):
        piece = lax.dynamic_index_in_dim(blocks, (rc + k) % cores, 1, keepdims=False)
        half = half + lax.ppermute(piece, "rc", [(i, (i + k) % cores) for i in range(cores)])
    total = lax.dynamic_index_in_dim(half, rx, 0, keepdims=False)
    for k in range(1, chips):
        piece = lax.dynamic_index_in_dim(half, (rx + k) % chips, 0, keepdims=False)
        total = total + lax.ppermute(piece, "rx", [(i, (i + k) % chips) for i in range(chips)])
    return total


def column_mass(kernel, row_scale):
    high = row_scale.astype(jnp.bfloat16)
    rest = row_scale - high.astype(jnp.float32)
    middle = rest.astype(jnp.bfloat16)
    low = (rest - middle.astype(jnp.float32)).astype(jnp.bfloat16)
    parts = jnp.stack([high, middle, low])
    return jnp.sum(jnp.dot(parts, kernel, preferred_element_type=jnp.float32), axis=0)


def row_step(kernel, col_scale, weights):
    partial_mass = jnp.sum(kernel.astype(jnp.float32) * col_scale[None, :], axis=1)
    masses = reduce_cent(partial_mass)
    return weights / masses


def per_device(vectors, centroids, weights):
    full_rows = lax.all_gather(vectors, CENT, axis=1, tiled=True)
    local_rows = full_rows.shape[0]
    feature_dimension = full_rows.shape[1]
    local_centres = centroids.shape[0]
    centre_total = local_centres * lax.axis_size(CENT)
    reciprocal_vector_magnitudes = lax.rsqrt(
        jnp.mean(jnp.square(full_rows.astype(jnp.float32)), axis=1) + 1e-06
    )
    reciprocal_centroid_magnitudes = lax.rsqrt(
        jnp.mean(jnp.square(centroids.astype(jnp.float32)), axis=1) + 1e-06
    )
    similarity_matrix = jnp.dot(full_rows, centroids.T, preferred_element_type=jnp.float32)
    sharpened_similarity = (
        similarity_matrix
        * reciprocal_vector_magnitudes[:, None]
        * reciprocal_centroid_magnitudes[None, :]
        / (feature_dimension * entropic_smoothing)
    )
    kernel = jnp.exp(sharpened_similarity).astype(jnp.bfloat16)
    col_scale = jnp.full((local_centres,), 1.0, jnp.float32) / centre_total
    row_scale = row_step(kernel, col_scale, weights)
    weight_sum = None
    for sweep in range(ITERS):
        partial_cols = column_mass(kernel, row_scale)
        if weight_sum is None:
            both = reduce_row(jnp.concatenate([partial_cols, jnp.sum(weights)[None]]))
            col_mass, weight_sum = both[:local_centres], both[local_centres]
        else:
            col_mass = reduce_row(partial_cols)
        col_scale = weight_sum / centre_total / col_mass
        row_scale = row_step(kernel, col_scale, weights)
    transport = (row_scale[:, None] * kernel.astype(jnp.float32) * col_scale[None, :]).astype(
        jnp.bfloat16
    )
    term = lax.dot_general(
        full_rows, transport, (((0,), (0,)), ((), ())), preferred_element_type=jnp.float32
    )
    own_summed = scatter_row(term)
    square_sum = reduce_row(jnp.sum(own_summed * own_summed, axis=0))
    new_centroids = own_summed * lax.rsqrt(square_sum / feature_dimension + 1e-06)[None, :]
    return (new_centroids, jnp.log(row_scale), jnp.log(centre_total * col_scale))


def solution(mesh):
    rows, cents = mesh.devices.shape
    split = Mesh(mesh.devices.reshape(rows // 2, 2, 4, cents // 4), ROW + CENT)
    return jax.shard_map(
        per_device,
        mesh=split,
        in_specs=(P(ROW, CENT), P(CENT, None), P(ROW)),
        out_specs=(P(ROW, CENT), P(ROW), P(CENT)),
        check_vma=False,
    )
```

```python
import jax
import jax.numpy as jnp
from jax import lax
from jax.sharding import Mesh
from jax.sharding import PartitionSpec as P

ITERS = 3


entropic_smoothing = 0.02

ROW = ("rx", "rc")
CENT = ("cy", "cz")


def shifted_sum(x, axis):
    n = lax.axis_size(axis)
    total = x
    for k in range(1, n):
        total = total + lax.ppermute(x, axis, [(i, (i + k) % n) for i in range(n)])
    return total


def reduce_cent(x):
    n = lax.axis_size(CENT)
    copies = lax.all_to_all(jnp.broadcast_to(x, (n, *x.shape)), CENT, 0, 0, tiled=False)
    return jnp.sum(copies, axis=0)


def reduce_row(x):
    return shifted_sum(shifted_sum(x, "rc"), "rx")


def scatter_row(x):
    chips, cores = lax.axis_size("rx"), lax.axis_size("rc")
    rx, rc = lax.axis_index("rx"), lax.axis_index("rc")
    blocks = x.reshape(chips, cores, x.shape[0] // (chips * cores), *x.shape[1:])
    half = lax.dynamic_index_in_dim(blocks, rc, 1, keepdims=False)
    for k in range(1, cores):
        piece = lax.dynamic_index_in_dim(blocks, (rc + k) % cores, 1, keepdims=False)
        half = half + lax.ppermute(piece, "rc", [(i, (i + k) % cores) for i in range(cores)])
    total = lax.dynamic_index_in_dim(half, rx, 0, keepdims=False)
    for k in range(1, chips):
        piece = lax.dynamic_index_in_dim(half, (rx + k) % chips, 0, keepdims=False)
        total = total + lax.ppermute(piece, "rx", [(i, (i + k) % chips) for i in range(chips)])
    return total


def gather_features(vectors):
    n = lax.axis_size(CENT)
    blocks = lax.all_to_all(
        jnp.broadcast_to(vectors, (n, *vectors.shape)), CENT, 0, 0, tiled=False
    )
    return jnp.transpose(blocks, (1, 0, 2)).reshape(vectors.shape[0], -1)


def row_step(kernel, col_scale, weights):
    partial_mass = jnp.sum(kernel.astype(jnp.float32) * col_scale[None, :], axis=1)
    masses = reduce_cent(partial_mass)
    return weights / masses


def per_device(vectors, centroids, weights):
    full_rows = gather_features(vectors)
    local_rows = full_rows.shape[0]
    feature_dimension = full_rows.shape[1]
    local_centres = centroids.shape[0]
    centre_total = local_centres * lax.axis_size(CENT)
    reciprocal_vector_magnitudes = lax.rsqrt(
        jnp.mean(jnp.square(full_rows.astype(jnp.float32)), axis=1) + 1e-06
    )
    reciprocal_centroid_magnitudes = lax.rsqrt(
        jnp.mean(jnp.square(centroids.astype(jnp.float32)), axis=1) + 1e-06
    )
    similarity_matrix = jnp.dot(full_rows, centroids.T, preferred_element_type=jnp.float32)
    sharpened_similarity = (
        similarity_matrix
        * reciprocal_vector_magnitudes[:, None]
        * reciprocal_centroid_magnitudes[None, :]
        / (feature_dimension * entropic_smoothing)
    )
    kernel = jnp.exp(sharpened_similarity).astype(jnp.bfloat16)
    col_scale = jnp.full((local_centres,), 1.0, jnp.float32) / centre_total
    row_scale = row_step(kernel, col_scale, weights)
    weight_sum = None
    for sweep in range(ITERS):
        partial_cols = jnp.sum(kernel.astype(jnp.float32) * row_scale[:, None], axis=0)
        if weight_sum is None:
            both = reduce_row(jnp.concatenate([partial_cols, jnp.sum(weights)[None]]))
            col_mass, weight_sum = both[:local_centres], both[local_centres]
        else:
            col_mass = reduce_row(partial_cols)
        col_scale = weight_sum / centre_total / col_mass
        row_scale = row_step(kernel, col_scale, weights)
    transport = (row_scale[:, None] * kernel.astype(jnp.float32) * col_scale[None, :]).astype(
        jnp.bfloat16
    )
    term = lax.dot_general(
        full_rows, transport, (((0,), (0,)), ((), ())), preferred_element_type=jnp.float32
    )
    own_summed = scatter_row(term)
    square_sum = reduce_row(jnp.sum(own_summed * own_summed, axis=0))
    new_centroids = own_summed * lax.rsqrt(square_sum / feature_dimension + 1e-06)[None, :]
    return (new_centroids, jnp.log(row_scale), jnp.log(centre_total * col_scale))


def solution(mesh):
    rows, cents = mesh.devices.shape
    split = Mesh(mesh.devices.reshape(rows // 2, 2, 4, cents // 4), ROW + CENT)
    return jax.shard_map(
        per_device,
        mesh=split,
        in_specs=(P(ROW, CENT), P(CENT, None), P(ROW)),
        out_specs=(P(ROW, CENT), P(ROW), P(CENT)),
        check_vma=False,
    )
```

```python
import jax
import jax.numpy as jnp
from jax import lax
from jax.sharding import Mesh
from jax.sharding import PartitionSpec as P

ITERS = 3


entropic_smoothing = 0.02

ROW = ("rx", "rc")
CENT = ("cy", "cz")


def shifted_sum(x, axis):
    n = lax.axis_size(axis)
    total = x
    for k in range(1, n):
        total = total + lax.ppermute(x, axis, [(i, (i + k) % n) for i in range(n)])
    return total


def reduce_cent(x):
    n = lax.axis_size(CENT)
    copies = lax.all_to_all(jnp.broadcast_to(x, (n, *x.shape)), CENT, 0, 0, tiled=False)
    return jnp.sum(copies, axis=0)


def reduce_row(x):
    return shifted_sum(shifted_sum(x, "rc"), "rx")


def summed_block(full_rows, transport):
    chips, cores = lax.axis_size("rx"), lax.axis_size("rc")
    rx, rc = lax.axis_index("rx"), lax.axis_index("rc")
    rows, features = full_rows.shape
    block = features // (chips * cores)
    by_core = full_rows.reshape(rows, chips, cores, block)

    def product(core):
        part = lax.dynamic_index_in_dim(by_core, core, 2, keepdims=False)
        return lax.dot_general(
            part, transport, (((0,), (0,)), ((), ())), preferred_element_type=jnp.float32
        )

    sent = product((rc + 1) % cores)
    received = lax.ppermute(sent, "rc", [(i, (i + 1) % cores) for i in range(cores)])
    half = lax.optimization_barrier(product(rc)) + received
    total = lax.dynamic_index_in_dim(half, rx, 0, keepdims=False)
    for k in range(1, chips):
        piece = lax.dynamic_index_in_dim(half, (rx + k) % chips, 0, keepdims=False)
        total = total + lax.ppermute(piece, "rx", [(i, (i + k) % chips) for i in range(chips)])
    return total


def gather_features(vectors):
    n = lax.axis_size(CENT)
    blocks = lax.all_to_all(
        jnp.broadcast_to(vectors, (n, *vectors.shape)), CENT, 0, 0, tiled=False
    )
    return jnp.transpose(blocks, (1, 0, 2)).reshape(vectors.shape[0], -1)


def row_step(kernel, col_scale, weights):
    partial_mass = jnp.sum(kernel.astype(jnp.float32) * col_scale[None, :], axis=1)
    masses = reduce_cent(partial_mass)
    return weights / masses


def per_device(vectors, centroids, weights):
    full_rows = gather_features(vectors)
    local_rows = full_rows.shape[0]
    feature_dimension = full_rows.shape[1]
    local_centres = centroids.shape[0]
    centre_total = local_centres * lax.axis_size(CENT)
    reciprocal_vector_magnitudes = lax.rsqrt(
        jnp.mean(jnp.square(full_rows.astype(jnp.float32)), axis=1) + 1e-06
    )
    reciprocal_centroid_magnitudes = lax.rsqrt(
        jnp.mean(jnp.square(centroids.astype(jnp.float32)), axis=1) + 1e-06
    )
    similarity_matrix = jnp.dot(full_rows, centroids.T, preferred_element_type=jnp.float32)
    sharpened_similarity = (
        similarity_matrix
        * reciprocal_vector_magnitudes[:, None]
        * reciprocal_centroid_magnitudes[None, :]
        / (feature_dimension * entropic_smoothing)
    )
    kernel = jnp.exp(sharpened_similarity).astype(jnp.bfloat16)
    col_scale = jnp.full((local_centres,), 1.0, jnp.float32) / centre_total
    row_scale = row_step(kernel, col_scale, weights)
    weight_sum = None
    for sweep in range(ITERS):
        partial_cols = jnp.sum(kernel.astype(jnp.float32) * row_scale[:, None], axis=0)
        if weight_sum is None:
            both = reduce_row(jnp.concatenate([partial_cols, jnp.sum(weights)[None]]))
            col_mass, weight_sum = both[:local_centres], both[local_centres]
        else:
            col_mass = reduce_row(partial_cols)
        col_scale = weight_sum / centre_total / col_mass
        row_scale = row_step(kernel, col_scale, weights)
    transport = (row_scale[:, None] * kernel.astype(jnp.float32) * col_scale[None, :]).astype(
        jnp.bfloat16
    )
    own_summed = summed_block(full_rows, transport)
    square_sum = reduce_row(jnp.sum(own_summed * own_summed, axis=0))
    new_centroids = own_summed * lax.rsqrt(square_sum / feature_dimension + 1e-06)[None, :]
    return (new_centroids, jnp.log(row_scale), jnp.log(centre_total * col_scale))


def solution(mesh):
    rows, cents = mesh.devices.shape
    split = Mesh(mesh.devices.reshape(rows // 2, 2, 4, cents // 4), ROW + CENT)
    return jax.shard_map(
        per_device,
        mesh=split,
        in_specs=(P(ROW, CENT), P(CENT, None), P(ROW)),
        out_specs=(P(ROW, CENT), P(ROW), P(CENT)),
        check_vma=False,
    )
```

```python
import jax
import jax.numpy as jnp
from jax import lax
from jax.sharding import Mesh
from jax.sharding import PartitionSpec as P

ITERS = 3


entropic_smoothing = 0.02

ROW = ("rx", "rc")
CENT = ("cy", "cz")


def shifted_sum(x, axis):
    n = lax.axis_size(axis)
    total = x
    for k in range(1, n):
        total = total + lax.ppermute(x, axis, [(i, (i + k) % n) for i in range(n)])
    return total


def reduce_cent(x):
    n = lax.axis_size(CENT)
    copies = lax.all_to_all(jnp.broadcast_to(x, (n, *x.shape)), CENT, 0, 0, tiled=False)
    return jnp.sum(copies, axis=0)


def reduce_row(x):
    return shifted_sum(shifted_sum(x, "rc"), "rx")


def summed_block(full_rows, transport):
    chips, cores = lax.axis_size("rx"), lax.axis_size("rc")
    rx, rc = lax.axis_index("rx"), lax.axis_index("rc")
    rows, features = full_rows.shape
    block = features // (chips * cores)
    by_core = full_rows.reshape(rows, chips, cores, block)

    def product(core):
        part = lax.dynamic_index_in_dim(by_core, core, 2, keepdims=False)
        return lax.dot_general(
            part, transport, (((0,), (0,)), ((), ())), preferred_element_type=jnp.float32
        )

    sent = product((rc + 1) % cores)
    received = lax.ppermute(sent, "rc", [(i, (i + 1) % cores) for i in range(cores)])
    half = lax.optimization_barrier(product(rc)) + received
    total = lax.dynamic_index_in_dim(half, rx, 0, keepdims=False)
    for k in range(1, chips):
        piece = lax.dynamic_index_in_dim(half, (rx + k) % chips, 0, keepdims=False)
        total = total + lax.ppermute(piece, "rx", [(i, (i + k) % chips) for i in range(chips)])
    return total


def gather_features(vectors):
    n = lax.axis_size(CENT)
    blocks = lax.all_to_all(
        jnp.broadcast_to(vectors, (n, *vectors.shape)), CENT, 0, 0, tiled=False
    )
    return jnp.transpose(blocks, (1, 0, 2)).reshape(vectors.shape[0], -1)


def row_step(kernel, col_scale, weights):
    partial_mass = jnp.sum(kernel.astype(jnp.float32) * col_scale[None, :], axis=1)
    masses = reduce_cent(partial_mass)
    return weights / masses


def per_device(vectors, centroids, weights):
    full_rows = gather_features(vectors)
    local_rows = full_rows.shape[0]
    feature_dimension = full_rows.shape[1]
    local_centres = centroids.shape[0]
    centre_total = local_centres * lax.axis_size(CENT)
    reciprocal_vector_magnitudes = lax.rsqrt(
        jnp.mean(jnp.square(full_rows.astype(jnp.float32)), axis=1) + 1e-06
    )
    reciprocal_centroid_magnitudes = lax.rsqrt(
        jnp.mean(jnp.square(centroids.astype(jnp.float32)), axis=1) + 1e-06
    )
    similarity_matrix = jnp.dot(full_rows, centroids.T, preferred_element_type=jnp.float32)
    sharpened_similarity = (
        similarity_matrix
        * reciprocal_vector_magnitudes[:, None]
        * reciprocal_centroid_magnitudes[None, :]
        / (feature_dimension * entropic_smoothing)
    )
    kernel = jnp.exp(sharpened_similarity).astype(jnp.bfloat16)
    col_scale = jnp.full((local_centres,), 1.0, jnp.float32) / centre_total
    row_scale = row_step(kernel, col_scale, weights)
    weight_sum = None
    for sweep in range(ITERS):
        partial_cols = jnp.sum(kernel.astype(jnp.float32) * row_scale[:, None], axis=0)
        if weight_sum is None:
            both = reduce_row(jnp.concatenate([partial_cols, jnp.sum(weights)[None]]))
            col_mass, weight_sum = both[:local_centres], both[local_centres]
        else:
            col_mass = reduce_row(partial_cols)
        col_scale = weight_sum / centre_total / col_mass
        row_scale = row_step(kernel, col_scale, weights)
    transport = (row_scale[:, None] * kernel.astype(jnp.float32) * col_scale[None, :]).astype(
        jnp.bfloat16
    )
    own_summed = summed_block(full_rows, lax.optimization_barrier(transport))
    square_sum = reduce_row(jnp.sum(own_summed * own_summed, axis=0))
    new_centroids = own_summed * lax.rsqrt(square_sum / feature_dimension + 1e-06)[None, :]
    return (new_centroids, jnp.log(row_scale), jnp.log(centre_total * col_scale))


def solution(mesh):
    rows, cents = mesh.devices.shape
    split = Mesh(mesh.devices.reshape(rows // 2, 2, 4, cents // 4), ROW + CENT)
    return jax.shard_map(
        per_device,
        mesh=split,
        in_specs=(P(ROW, CENT), P(CENT, None), P(ROW)),
        out_specs=(P(ROW, CENT), P(ROW), P(CENT)),
        check_vma=False,
    )
```

```python
import jax
import jax.numpy as jnp
from jax import lax
from jax.sharding import Mesh
from jax.sharding import PartitionSpec as P

ITERS = 3


entropic_smoothing = 0.02

ROW = ("rx", "rc")
CENT = ("cy", "cz")


def shifted_sum(x, axis):
    n = lax.axis_size(axis)
    total = x
    for k in range(1, n):
        total = total + lax.ppermute(x, axis, [(i, (i + k) % n) for i in range(n)])
    return total


def reduce_cent(x):
    n = lax.axis_size(CENT)
    copies = lax.all_to_all(jnp.broadcast_to(x, (n, *x.shape)), CENT, 0, 0, tiled=False)
    return jnp.sum(copies, axis=0)


def reduce_row(x):
    return shifted_sum(shifted_sum(x, "rc"), "rx")


def summed_block(full_rows, transport):
    chips, cores = lax.axis_size("rx"), lax.axis_size("rc")
    rx, rc = lax.axis_index("rx"), lax.axis_index("rc")
    rows, features = full_rows.shape
    block = features // (chips * cores)
    by_core = full_rows.reshape(rows, chips, cores, block)

    def product(core):
        part = lax.dynamic_index_in_dim(by_core, core, 2, keepdims=False)
        return lax.dot_general(
            part, transport, (((0,), (0,)), ((), ())), preferred_element_type=jnp.float32
        )

    sent = product((rc + 1) % cores)
    received = lax.ppermute(sent, "rc", [(i, (i + 1) % cores) for i in range(cores)])
    half = lax.optimization_barrier(product(rc)) + received
    split = block // 2
    clockwise = ring_sum(half[:, :split], rx, chips, 1)
    counter = ring_sum(half[:, split:], rx, chips, -1)
    return jnp.concatenate([clockwise, counter], axis=0)


def ring_sum(blocks, me, n, step):
    neighbour = [(i, (i + step) % n) for i in range(n)]
    total = lax.dynamic_index_in_dim(blocks, (me - step) % n, 0, keepdims=False)
    for s in range(1, n):
        arrived = lax.ppermute(total, "rx", neighbour)
        own = lax.dynamic_index_in_dim(blocks, (me - step * (1 + s)) % n, 0, keepdims=False)
        total = arrived + own
    return total


def gather_features(vectors):
    n = lax.axis_size(CENT)
    blocks = lax.all_to_all(
        jnp.broadcast_to(vectors, (n, *vectors.shape)), CENT, 0, 0, tiled=False
    )
    return jnp.transpose(blocks, (1, 0, 2)).reshape(vectors.shape[0], -1)


def row_step(kernel, col_scale, weights):
    partial_mass = jnp.sum(kernel.astype(jnp.float32) * col_scale[None, :], axis=1)
    masses = reduce_cent(partial_mass)
    return weights / masses


def per_device(vectors, centroids, weights):
    full_rows = gather_features(vectors)
    local_rows = full_rows.shape[0]
    feature_dimension = full_rows.shape[1]
    local_centres = centroids.shape[0]
    centre_total = local_centres * lax.axis_size(CENT)
    reciprocal_vector_magnitudes = lax.rsqrt(
        jnp.mean(jnp.square(full_rows.astype(jnp.float32)), axis=1) + 1e-06
    )
    reciprocal_centroid_magnitudes = lax.rsqrt(
        jnp.mean(jnp.square(centroids.astype(jnp.float32)), axis=1) + 1e-06
    )
    similarity_matrix = jnp.dot(full_rows, centroids.T, preferred_element_type=jnp.float32)
    sharpened_similarity = (
        similarity_matrix
        * reciprocal_vector_magnitudes[:, None]
        * reciprocal_centroid_magnitudes[None, :]
        / (feature_dimension * entropic_smoothing)
    )
    kernel = jnp.exp(sharpened_similarity).astype(jnp.bfloat16)
    col_scale = jnp.full((local_centres,), 1.0, jnp.float32) / centre_total
    row_scale = row_step(kernel, col_scale, weights)
    weight_sum = None
    for sweep in range(ITERS):
        partial_cols = jnp.sum(kernel.astype(jnp.float32) * row_scale[:, None], axis=0)
        if weight_sum is None:
            both = reduce_row(jnp.concatenate([partial_cols, jnp.sum(weights)[None]]))
            col_mass, weight_sum = both[:local_centres], both[local_centres]
        else:
            col_mass = reduce_row(partial_cols)
        col_scale = weight_sum / centre_total / col_mass
        row_scale = row_step(kernel, col_scale, weights)
    transport = (row_scale[:, None] * kernel.astype(jnp.float32) * col_scale[None, :]).astype(
        jnp.bfloat16
    )
    own_summed = summed_block(full_rows, transport)
    square_sum = reduce_row(jnp.sum(own_summed * own_summed, axis=0))
    new_centroids = own_summed * lax.rsqrt(square_sum / feature_dimension + 1e-06)[None, :]
    return (new_centroids, jnp.log(row_scale), jnp.log(centre_total * col_scale))


def solution(mesh):
    rows, cents = mesh.devices.shape
    split = Mesh(mesh.devices.reshape(rows // 2, 2, 4, cents // 4), ROW + CENT)
    return jax.shard_map(
        per_device,
        mesh=split,
        in_specs=(P(ROW, CENT), P(CENT, None), P(ROW)),
        out_specs=(P(ROW, CENT), P(ROW), P(CENT)),
        check_vma=False,
    )
```

```python
import jax
import jax.numpy as jnp
from jax import lax
from jax.sharding import Mesh
from jax.sharding import PartitionSpec as P

ITERS = 3


entropic_smoothing = 0.02

ROW = ("rx", "rc")
CENT = ("cy", "cz")


def shifted_sum(x, axis):
    n = lax.axis_size(axis)
    total = x
    for k in range(1, n):
        total = total + lax.ppermute(x, axis, [(i, (i + k) % n) for i in range(n)])
    return total


def reduce_cent(x):
    n = lax.axis_size(CENT)
    copies = lax.all_to_all(jnp.broadcast_to(x, (n, *x.shape)), CENT, 0, 0, tiled=False)
    return jnp.sum(copies, axis=0)


def reduce_row(x):
    return shifted_sum(shifted_sum(x, "rc"), "rx")


def gather_sum_row(x):
    n = lax.axis_size(ROW)
    copies = lax.all_to_all(jnp.broadcast_to(x, (n, *x.shape)), ROW, 0, 0, tiled=False)
    return jnp.sum(copies, axis=0)


def summed_block(full_rows, transport):
    chips, cores = lax.axis_size("rx"), lax.axis_size("rc")
    rx, rc = lax.axis_index("rx"), lax.axis_index("rc")
    rows, features = full_rows.shape
    block = features // (chips * cores)
    by_core = full_rows.reshape(rows, chips, cores, block)

    def product(core):
        part = lax.dynamic_index_in_dim(by_core, core, 2, keepdims=False)
        return lax.dot_general(
            part, transport, (((0,), (0,)), ((), ())), preferred_element_type=jnp.float32
        )

    sent = product((rc + 1) % cores)
    received = lax.ppermute(sent, "rc", [(i, (i + 1) % cores) for i in range(cores)])
    half = lax.optimization_barrier(product(rc)) + received
    total = lax.dynamic_index_in_dim(half, rx, 0, keepdims=False)
    for k in range(1, chips):
        piece = lax.dynamic_index_in_dim(half, (rx + k) % chips, 0, keepdims=False)
        total = total + lax.ppermute(piece, "rx", [(i, (i + k) % chips) for i in range(chips)])
    return total


def gather_features(vectors):
    n = lax.axis_size(CENT)
    blocks = lax.all_to_all(
        jnp.broadcast_to(vectors, (n, *vectors.shape)), CENT, 0, 0, tiled=False
    )
    return jnp.transpose(blocks, (1, 0, 2)).reshape(vectors.shape[0], -1)


def row_step(kernel, col_scale, weights):
    partial_mass = jnp.sum(kernel.astype(jnp.float32) * col_scale[None, :], axis=1)
    masses = reduce_cent(partial_mass)
    return weights / masses


def per_device(vectors, centroids, weights):
    full_rows = gather_features(vectors)
    local_rows = full_rows.shape[0]
    feature_dimension = full_rows.shape[1]
    local_centres = centroids.shape[0]
    centre_total = local_centres * lax.axis_size(CENT)
    reciprocal_vector_magnitudes = lax.rsqrt(
        jnp.mean(jnp.square(full_rows.astype(jnp.float32)), axis=1) + 1e-06
    )
    reciprocal_centroid_magnitudes = lax.rsqrt(
        jnp.mean(jnp.square(centroids.astype(jnp.float32)), axis=1) + 1e-06
    )
    similarity_matrix = jnp.dot(full_rows, centroids.T, preferred_element_type=jnp.float32)
    sharpened_similarity = (
        similarity_matrix
        * reciprocal_vector_magnitudes[:, None]
        * reciprocal_centroid_magnitudes[None, :]
        / (feature_dimension * entropic_smoothing)
    )
    kernel = jnp.exp(sharpened_similarity).astype(jnp.bfloat16)
    col_scale = jnp.full((local_centres,), 1.0, jnp.float32) / centre_total
    row_scale = row_step(kernel, col_scale, weights)
    weight_sum = None
    for sweep in range(ITERS):
        partial_cols = jnp.sum(kernel.astype(jnp.float32) * row_scale[:, None], axis=0)
        if weight_sum is None:
            both = reduce_row(jnp.concatenate([partial_cols, jnp.sum(weights)[None]]))
            col_mass, weight_sum = both[:local_centres], both[local_centres]
        else:
            col_mass = reduce_row(partial_cols)
        col_scale = weight_sum / centre_total / col_mass
        row_scale = row_step(kernel, col_scale, weights)
    transport = (row_scale[:, None] * kernel.astype(jnp.float32) * col_scale[None, :]).astype(
        jnp.bfloat16
    )
    own_summed = summed_block(full_rows, transport)
    square_sum = gather_sum_row(jnp.sum(own_summed * own_summed, axis=0))
    new_centroids = own_summed * lax.rsqrt(square_sum / feature_dimension + 1e-06)[None, :]
    return (new_centroids, jnp.log(row_scale), jnp.log(centre_total * col_scale))


def solution(mesh):
    rows, cents = mesh.devices.shape
    split = Mesh(mesh.devices.reshape(rows // 2, 2, 4, cents // 4), ROW + CENT)
    return jax.shard_map(
        per_device,
        mesh=split,
        in_specs=(P(ROW, CENT), P(CENT, None), P(ROW)),
        out_specs=(P(ROW, CENT), P(ROW), P(CENT)),
        check_vma=False,
    )
```

```python
import jax
import jax.numpy as jnp
from jax import lax
from jax.sharding import Mesh
from jax.sharding import PartitionSpec as P

ITERS = 3


entropic_smoothing = 0.02

ROW = ("rx", "rc")
CENT = ("cy", "cz")


def shifted_sum(x, axis):
    n = lax.axis_size(axis)
    total = x
    for k in range(1, n):
        total = total + lax.ppermute(x, axis, [(i, (i + k) % n) for i in range(n)])
    return total


def reduce_cent(x):
    n = lax.axis_size(CENT)
    copies = lax.all_to_all(jnp.broadcast_to(x, (n, *x.shape)), CENT, 0, 0, tiled=False)
    return jnp.sum(copies, axis=0)


def reduce_row(x):
    return shifted_sum(shifted_sum(x, "rc"), "rx")


def summed_block(full_rows, transport):
    chips, cores = lax.axis_size("rx"), lax.axis_size("rc")
    rx, rc = lax.axis_index("rx"), lax.axis_index("rc")
    rows, features = full_rows.shape
    block = features // (chips * cores)
    by_core = full_rows.reshape(rows, chips, cores, block)

    def product(core):
        part = lax.dynamic_index_in_dim(by_core, core, 2, keepdims=False)
        return lax.dot_general(
            part, transport, (((0,), (0,)), ((), ())), preferred_element_type=jnp.float32
        )

    sent = product((rc + 1) % cores)
    received = lax.ppermute(sent, "rc", [(i, (i + 1) % cores) for i in range(cores)])
    half = lax.optimization_barrier(product(rc)) + received
    total = lax.dynamic_index_in_dim(half, rx, 0, keepdims=False)
    for k in range(1, chips):
        piece = lax.dynamic_index_in_dim(half, (rx + k) % chips, 0, keepdims=False)
        total = total + lax.ppermute(piece, "rx", [(i, (i + k) % chips) for i in range(chips)])
    return total


def gather_features(vectors):
    n = lax.axis_size(CENT)
    blocks = lax.all_to_all(
        jnp.broadcast_to(vectors, (n, *vectors.shape)), CENT, 0, 0, tiled=False
    )
    return jnp.transpose(blocks, (1, 0, 2)).reshape(vectors.shape[0], -1)


def row_step(kernel, col_scale, weights):
    partial_mass = jnp.sum(kernel.astype(jnp.float32) * col_scale[None, :], axis=1)
    masses = reduce_cent(partial_mass)
    return weights / masses


def per_device(vectors, centroids, weights):
    full_rows = gather_features(vectors)
    local_rows = full_rows.shape[0]
    feature_dimension = full_rows.shape[1]
    local_centres = centroids.shape[0]
    centre_total = local_centres * lax.axis_size(CENT)
    reciprocal_vector_magnitudes = lax.rsqrt(
        jnp.mean(jnp.square(full_rows.astype(jnp.float32)), axis=1) + 1e-06
    )
    reciprocal_centroid_magnitudes = lax.rsqrt(
        jnp.mean(jnp.square(centroids.astype(jnp.float32)), axis=1) + 1e-06
    )
    weight_sum, reciprocal_centroid_magnitudes = lax.optimization_barrier(
        (reduce_row(jnp.sum(weights)), reciprocal_centroid_magnitudes)
    )
    similarity_matrix = jnp.dot(full_rows, centroids.T, preferred_element_type=jnp.float32)
    sharpened_similarity = (
        similarity_matrix
        * reciprocal_vector_magnitudes[:, None]
        * reciprocal_centroid_magnitudes[None, :]
        / (feature_dimension * entropic_smoothing)
    )
    kernel = jnp.exp(sharpened_similarity).astype(jnp.bfloat16)
    col_scale = jnp.full((local_centres,), 1.0, jnp.float32) / centre_total
    row_scale = row_step(kernel, col_scale, weights)
    for sweep in range(ITERS):
        partial_cols = jnp.sum(kernel.astype(jnp.float32) * row_scale[:, None], axis=0)
        col_mass = reduce_row(partial_cols)
        col_scale = weight_sum / centre_total / col_mass
        row_scale = row_step(kernel, col_scale, weights)
    transport = (row_scale[:, None] * kernel.astype(jnp.float32) * col_scale[None, :]).astype(
        jnp.bfloat16
    )
    own_summed = summed_block(full_rows, transport)
    square_sum = reduce_row(jnp.sum(own_summed * own_summed, axis=0))
    new_centroids = own_summed * lax.rsqrt(square_sum / feature_dimension + 1e-06)[None, :]
    return (new_centroids, jnp.log(row_scale), jnp.log(centre_total * col_scale))


def solution(mesh):
    rows, cents = mesh.devices.shape
    split = Mesh(mesh.devices.reshape(rows // 2, 2, 4, cents // 4), ROW + CENT)
    return jax.shard_map(
        per_device,
        mesh=split,
        in_specs=(P(ROW, CENT), P(CENT, None), P(ROW)),
        out_specs=(P(ROW, CENT), P(ROW), P(CENT)),
        check_vma=False,
    )
```

```python
import jax
import jax.numpy as jnp
from jax import lax
from jax.sharding import Mesh
from jax.sharding import PartitionSpec as P

ITERS = 3


entropic_smoothing = 0.02

ROW = ("rx", "rc")
CENT = ("cy", "cz")


def shifted_sum(x, axis):
    n = lax.axis_size(axis)
    total = x
    for k in range(1, n):
        total = total + lax.ppermute(x, axis, [(i, (i + k) % n) for i in range(n)])
    return total


def reduce_cent(x):
    n = lax.axis_size(CENT)
    copies = lax.all_to_all(jnp.broadcast_to(x, (n, *x.shape)), CENT, 0, 0, tiled=False)
    return jnp.sum(copies, axis=0)


def reduce_row(x):
    return shifted_sum(shifted_sum(x, "rc"), "rx")


def summed_block(full_rows, transport):
    chips, cores = lax.axis_size("rx"), lax.axis_size("rc")
    rx, rc = lax.axis_index("rx"), lax.axis_index("rc")
    rows, features = full_rows.shape
    block = features // (chips * cores)
    by_core = full_rows.reshape(rows, chips, cores, block)

    def product(core):
        part = lax.dynamic_index_in_dim(by_core, core, 2, keepdims=False)
        return lax.dot_general(
            part, transport, (((0,), (0,)), ((), ())), preferred_element_type=jnp.float32
        )

    sent = product((rc + 1) % cores)
    received = lax.ppermute(sent, "rc", [(i, (i + 1) % cores) for i in range(cores)])
    half = lax.optimization_barrier(product(rc)) + received
    total = lax.dynamic_index_in_dim(half, rx, 0, keepdims=False)
    for k in range(1, chips):
        piece = lax.dynamic_index_in_dim(half, (rx + k) % chips, 0, keepdims=False)
        total = total + lax.ppermute(piece, "rx", [(i, (i + k) % chips) for i in range(chips)])
    return total


def gather_features(vectors):
    n = lax.axis_size(CENT)
    blocks = lax.all_to_all(
        jnp.broadcast_to(vectors, (n, *vectors.shape)), CENT, 0, 0, tiled=False
    )
    return jnp.transpose(blocks, (1, 0, 2)).reshape(vectors.shape[0], -1)


def column_mass(kernel, row_scale):
    rows, cols = kernel.shape
    grouped = kernel.reshape(rows // 128, 128, cols).astype(jnp.float32)
    lanes = jnp.sum(grouped * row_scale.reshape(rows // 128, 128, 1), axis=0)
    return jnp.sum(lax.optimization_barrier(lanes), axis=0)


def row_step(kernel, col_scale, weights):
    partial_mass = jnp.sum(kernel.astype(jnp.float32) * col_scale[None, :], axis=1)
    masses = reduce_cent(partial_mass)
    return weights / masses


def per_device(vectors, centroids, weights):
    full_rows = gather_features(vectors)
    local_rows = full_rows.shape[0]
    feature_dimension = full_rows.shape[1]
    local_centres = centroids.shape[0]
    centre_total = local_centres * lax.axis_size(CENT)
    reciprocal_vector_magnitudes = lax.rsqrt(
        jnp.mean(jnp.square(full_rows.astype(jnp.float32)), axis=1) + 1e-06
    )
    reciprocal_centroid_magnitudes = lax.rsqrt(
        jnp.mean(jnp.square(centroids.astype(jnp.float32)), axis=1) + 1e-06
    )
    weight_sum, reciprocal_centroid_magnitudes = lax.optimization_barrier(
        (reduce_row(jnp.sum(weights)), reciprocal_centroid_magnitudes)
    )
    similarity_matrix = jnp.dot(full_rows, centroids.T, preferred_element_type=jnp.float32)
    sharpened_similarity = (
        similarity_matrix
        * reciprocal_vector_magnitudes[:, None]
        * reciprocal_centroid_magnitudes[None, :]
        / (feature_dimension * entropic_smoothing)
    )
    kernel = jnp.exp(sharpened_similarity).astype(jnp.bfloat16)
    col_scale = jnp.full((local_centres,), 1.0, jnp.float32) / centre_total
    row_scale = row_step(kernel, col_scale, weights)
    for sweep in range(ITERS):
        partial_cols = column_mass(kernel, row_scale)
        col_mass = reduce_row(partial_cols)
        col_scale = weight_sum / centre_total / col_mass
        row_scale = row_step(kernel, col_scale, weights)
    transport = (row_scale[:, None] * kernel.astype(jnp.float32) * col_scale[None, :]).astype(
        jnp.bfloat16
    )
    own_summed = summed_block(full_rows, transport)
    square_sum = reduce_row(jnp.sum(own_summed * own_summed, axis=0))
    new_centroids = own_summed * lax.rsqrt(square_sum / feature_dimension + 1e-06)[None, :]
    return (new_centroids, jnp.log(row_scale), jnp.log(centre_total * col_scale))


def solution(mesh):
    rows, cents = mesh.devices.shape
    split = Mesh(mesh.devices.reshape(rows // 2, 2, 4, cents // 4), ROW + CENT)
    return jax.shard_map(
        per_device,
        mesh=split,
        in_specs=(P(ROW, CENT), P(CENT, None), P(ROW)),
        out_specs=(P(ROW, CENT), P(ROW), P(CENT)),
        check_vma=False,
    )
```

```python
import jax
import jax.numpy as jnp
from jax import lax
from jax.sharding import Mesh
from jax.sharding import PartitionSpec as P

ITERS = 3


entropic_smoothing = 0.02

ROW = ("rx", "rc")
CENT = ("cy", "cz")


def shifted_sum(x, axis):
    n = lax.axis_size(axis)
    total = x
    for k in range(1, n):
        total = total + lax.ppermute(x, axis, [(i, (i + k) % n) for i in range(n)])
    return total


def reduce_cent(x):
    n = lax.axis_size(CENT)
    copies = lax.all_to_all(jnp.broadcast_to(x, (n, *x.shape)), CENT, 0, 0, tiled=False)
    return jnp.sum(copies, axis=0)


def reduce_row(x):
    return shifted_sum(shifted_sum(x, "rc"), "rx")


def summed_block(full_rows, transport):
    chips, cores = lax.axis_size("rx"), lax.axis_size("rc")
    rx, rc = lax.axis_index("rx"), lax.axis_index("rc")
    rows, features = full_rows.shape
    block = features // (chips * cores)
    by_core = full_rows.reshape(rows, chips, cores, block)

    def product(core):
        part = lax.dynamic_index_in_dim(by_core, core, 2, keepdims=False)
        return lax.dot_general(
            part, transport, (((0,), (0,)), ((), ())), preferred_element_type=jnp.float32
        )

    sent = product((rc + 1) % cores)
    received = lax.ppermute(sent, "rc", [(i, (i + 1) % cores) for i in range(cores)])
    kept = lax.optimization_barrier(product(rc))

    def half_block(chip):
        return lax.dynamic_index_in_dim(kept, chip, 0, keepdims=False) + (
            lax.dynamic_index_in_dim(received, chip, 0, keepdims=False)
        )

    total = half_block(rx)
    for k in range(1, chips):
        piece = half_block((rx + k) % chips)
        total = total + lax.ppermute(piece, "rx", [(i, (i + k) % chips) for i in range(chips)])
    return total


def gather_features(vectors):
    n = lax.axis_size(CENT)
    blocks = lax.all_to_all(
        jnp.broadcast_to(vectors, (n, *vectors.shape)), CENT, 0, 0, tiled=False
    )
    return jnp.transpose(blocks, (1, 0, 2)).reshape(vectors.shape[0], -1)


def row_step(kernel, col_scale, weights):
    partial_mass = jnp.sum(kernel.astype(jnp.float32) * col_scale[None, :], axis=1)
    masses = reduce_cent(partial_mass)
    return weights / masses


def per_device(vectors, centroids, weights):
    full_rows = gather_features(vectors)
    local_rows = full_rows.shape[0]
    feature_dimension = full_rows.shape[1]
    local_centres = centroids.shape[0]
    centre_total = local_centres * lax.axis_size(CENT)
    reciprocal_vector_magnitudes = lax.rsqrt(
        jnp.mean(jnp.square(full_rows.astype(jnp.float32)), axis=1) + 1e-06
    )
    reciprocal_centroid_magnitudes = lax.rsqrt(
        jnp.mean(jnp.square(centroids.astype(jnp.float32)), axis=1) + 1e-06
    )
    weight_sum, reciprocal_centroid_magnitudes = lax.optimization_barrier(
        (reduce_row(jnp.sum(weights)), reciprocal_centroid_magnitudes)
    )
    similarity_matrix = jnp.dot(full_rows, centroids.T, preferred_element_type=jnp.float32)
    sharpened_similarity = (
        similarity_matrix
        * reciprocal_vector_magnitudes[:, None]
        * reciprocal_centroid_magnitudes[None, :]
        / (feature_dimension * entropic_smoothing)
    )
    kernel = jnp.exp(sharpened_similarity).astype(jnp.bfloat16)
    col_scale = jnp.full((local_centres,), 1.0, jnp.float32) / centre_total
    row_scale = row_step(kernel, col_scale, weights)
    for sweep in range(ITERS):
        partial_cols = jnp.sum(kernel.astype(jnp.float32) * row_scale[:, None], axis=0)
        col_mass = reduce_row(partial_cols)
        col_scale = weight_sum / centre_total / col_mass
        row_scale = row_step(kernel, col_scale, weights)
    transport = (row_scale[:, None] * kernel.astype(jnp.float32) * col_scale[None, :]).astype(
        jnp.bfloat16
    )
    own_summed = summed_block(full_rows, transport)
    square_sum = reduce_row(jnp.sum(own_summed * own_summed, axis=0))
    new_centroids = own_summed * lax.rsqrt(square_sum / feature_dimension + 1e-06)[None, :]
    return (new_centroids, jnp.log(row_scale), jnp.log(centre_total * col_scale))


def solution(mesh):
    rows, cents = mesh.devices.shape
    split = Mesh(mesh.devices.reshape(rows // 2, 2, 4, cents // 4), ROW + CENT)
    return jax.shard_map(
        per_device,
        mesh=split,
        in_specs=(P(ROW, CENT), P(CENT, None), P(ROW)),
        out_specs=(P(ROW, CENT), P(ROW), P(CENT)),
        check_vma=False,
    )
```

```python
import jax
import jax.numpy as jnp
from jax import lax
from jax.sharding import Mesh
from jax.sharding import PartitionSpec as P

ITERS = 3


entropic_smoothing = 0.02

ROW = ("rx", "rc")
CENT = ("cy", "cz")


def shifted_sum(x, axis):
    n = lax.axis_size(axis)
    total = x
    for k in range(1, n):
        total = total + lax.ppermute(x, axis, [(i, (i + k) % n) for i in range(n)])
    return total


def reduce_cent(x):
    n = lax.axis_size(CENT)
    copies = lax.all_to_all(jnp.broadcast_to(x, (n, *x.shape)), CENT, 0, 0, tiled=False)
    return jnp.sum(copies, axis=0)


def reduce_row(x):
    return shifted_sum(shifted_sum(x, "rc"), "rx")


def summed_block(full_rows, transport):
    chips, cores = lax.axis_size("rx"), lax.axis_size("rc")
    rx, rc = lax.axis_index("rx"), lax.axis_index("rc")
    rows, features = full_rows.shape
    block = features // (chips * cores)
    by_core = full_rows.reshape(rows, chips, cores, block)

    def product(core):
        part = lax.dynamic_index_in_dim(by_core, core, 2, keepdims=False)
        return lax.dot_general(
            part, transport, (((0,), (0,)), ((), ())), preferred_element_type=jnp.float32
        )

    sent = product((rc + 1) % cores)
    received = lax.ppermute(sent, "rc", [(i, (i + 1) % cores) for i in range(cores)])
    half = lax.optimization_barrier(product(rc)) + received
    total = lax.dynamic_index_in_dim(half, rx, 0, keepdims=False)
    for k in range(1, chips):
        piece = lax.dynamic_index_in_dim(half, (rx + k) % chips, 0, keepdims=False)
        total = total + lax.ppermute(piece, "rx", [(i, (i + k) % chips) for i in range(chips)])
    return total


def gather_features(vectors):
    n = lax.axis_size(CENT)
    blocks = lax.all_to_all(
        jnp.broadcast_to(vectors, (n, *vectors.shape)), CENT, 0, 0, tiled=False
    )
    return jnp.transpose(blocks, (1, 0, 2)).reshape(vectors.shape[0], -1)


def row_step(kernel, col_scale, weights):
    partial_mass = jnp.sum(kernel.astype(jnp.float32) * col_scale[None, :], axis=1)
    masses = reduce_cent(partial_mass)
    return weights / masses


def per_device(vectors, centroids, weights):
    full_rows = gather_features(vectors)
    local_rows = full_rows.shape[0]
    feature_dimension = full_rows.shape[1]
    local_centres = centroids.shape[0]
    centre_total = local_centres * lax.axis_size(CENT)
    local_squares = jnp.sum(jnp.square(vectors.astype(jnp.float32)), axis=1)
    square_norms = shifted_sum(shifted_sum(local_squares, "cz"), "cy")
    reciprocal_centroid_magnitudes = lax.rsqrt(
        jnp.mean(jnp.square(centroids.astype(jnp.float32)), axis=1) + 1e-06
    )
    weight_sum, square_norms, reciprocal_centroid_magnitudes = lax.optimization_barrier(
        (reduce_row(jnp.sum(weights)), square_norms, reciprocal_centroid_magnitudes)
    )
    reciprocal_vector_magnitudes = lax.rsqrt(square_norms / feature_dimension + 1e-06)
    similarity_matrix = jnp.dot(full_rows, centroids.T, preferred_element_type=jnp.float32)
    sharpened_similarity = (
        similarity_matrix
        * reciprocal_vector_magnitudes[:, None]
        * reciprocal_centroid_magnitudes[None, :]
        / (feature_dimension * entropic_smoothing)
    )
    kernel = jnp.exp(sharpened_similarity).astype(jnp.bfloat16)
    col_scale = jnp.full((local_centres,), 1.0, jnp.float32) / centre_total
    row_scale = row_step(kernel, col_scale, weights)
    for sweep in range(ITERS):
        partial_cols = jnp.sum(kernel.astype(jnp.float32) * row_scale[:, None], axis=0)
        col_mass = reduce_row(partial_cols)
        col_scale = weight_sum / centre_total / col_mass
        row_scale = row_step(kernel, col_scale, weights)
    transport = (row_scale[:, None] * kernel.astype(jnp.float32) * col_scale[None, :]).astype(
        jnp.bfloat16
    )
    own_summed = summed_block(full_rows, transport)
    square_sum = reduce_row(jnp.sum(own_summed * own_summed, axis=0))
    new_centroids = own_summed * lax.rsqrt(square_sum / feature_dimension + 1e-06)[None, :]
    return (new_centroids, jnp.log(row_scale), jnp.log(centre_total * col_scale))


def solution(mesh):
    rows, cents = mesh.devices.shape
    split = Mesh(mesh.devices.reshape(rows // 2, 2, 4, cents // 4), ROW + CENT)
    return jax.shard_map(
        per_device,
        mesh=split,
        in_specs=(P(ROW, CENT), P(CENT, None), P(ROW)),
        out_specs=(P(ROW, CENT), P(ROW), P(CENT)),
        check_vma=False,
    )
```
